256 devices in a mesh: row: 16 (over z_hi, x, core), col: 16 (over y, z_lo).
Axes of the slice: x: 4, y: 4, z: 8 (z_hi: 2, z_lo: 4; z = z_hi * 4 + z_lo), core: 2. Of those that a mesh axis runs over, the one named last changes fastest.
Arguments:
- points: float32 [64, 32768], P(None, ('row', 'col')), may hold values from -24 to 24, as said below
- embedding: float32 [2, 32768], P(None, ('row', 'col')), may hold values from -8 to 8
- precision: float32 [32768], P(('row', 'col')), may hold values from 0.05 to 2
Outputs:
- force: float32 [2, 32768], P(None, ('row', 'col'))
- calibrated: float32 [32768], P(('row', 'col'))
The draws below stay inside these ranges and needn't reach their ends.
Inputs may be any that keep to these rules, and one draw needn't show every extreme that they name: `points`: each point's coordinates are normal values times a positive scale of that point.
All inputs are finite; a program needn't handle non-finite values.
Results may differ from the reference program's by a relative error of at most 0.0003.
Values sent between devices are 32-bit elements; how exact they have to be, the bound alone decides.
No kernel may reach another device: no remote copies, remote signals or barrier semaphores. Data moves between devices by JAX's collectives and lax.ppermute only.
A program may use at most 64 MiB of HBM per device.

```python
import math
import jax
import jax.numpy as jnp
from jax import lax

DIM = 64
PERP = 30
POINTS = 32768


def draw_points(key, part):
    first_key, second_key = jax.random.split(key)
    base = jnp.clip(jax.random.normal(first_key, (DIM, POINTS), jnp.float32), -6.0, 6.0)
    lowest, highest = (0.5, 2.0)
    scales = jnp.exp(jax.random.uniform(second_key, (1, POINTS), jnp.float32, math.log(lowest), math.log(highest)))
    return base * scales


def levels(own_key, extent, cuts, low, high):
    factor_of = 1.0
    for position, parts in cuts:
        steps = jax.random.uniform(jax.random.fold_in(jax.random.fold_in(own_key, 6), position), (parts,), jnp.float32, low / len(cuts), high / len(cuts))
        factor_of = factor_of * jnp.repeat(jnp.exp(steps), extent[position] // parts).reshape((-1,) + (1,) * (len(extent) - 1 - position))
    return factor_of


def noise(own_key, shape, scale, bound, shards=(), held_as=jnp.bfloat16):
    values = scale * jax.random.normal(own_key, shape, jnp.float32)
    if shards:
        values = values * levels(own_key, shape, shards, -0.22, 0.18)
    return jnp.clip(values, -bound, bound).astype(held_as)


def setup_inputs(seed: int = 0) -> dict:
    splits = jax.random.split(jax.random.key(seed), 4)
    points = draw_points(jax.random.fold_in(splits[3], 71), 0)
    embedding = noise(splits[1], (2, POINTS), 2.0, 8.0, ((1, 256),), jnp.float32)
    precision = jnp.clip(jnp.exp(math.log(2.0) - 3.6888794 * jax.random.uniform(splits[2], (POINTS,), jnp.float32) ** levels(splits[2], (POINTS,), ((0, 256),), -0.2, 0.2)), 0.05, 2.0)
    return dict(points=points, embedding=embedding, precision=precision)


def newton_update(zsum, first, second, start_prec):
    entropy = jnp.log(zsum) + start_prec * first / zsum
    spread = second / zsum - (first / zsum) ** 2
    factor = jnp.clip((entropy - math.log(PERP)) / jnp.maximum(start_prec * start_prec * spread, 1.0), -2.0, 2.0)
    return start_prec * jnp.exp(factor)


def reference(points, embedding, precision):
    coords = points.T
    total = coords.shape[0]
    sqsum = jnp.sum(coords * coords, axis=1)
    block_rows = min(total, 512)
    blocks = total // block_rows
    all_ids = jnp.arange(total, dtype=jnp.int32)
    starts = jnp.arange(blocks, dtype=jnp.int32) * block_rows

    def distances(start):
        part = lax.dynamic_slice_in_dim(coords, start, block_rows, 0)
        part_sq = lax.dynamic_slice_in_dim(sqsum, start, block_rows, 0)
        inner = jnp.dot(part, coords.T, precision=lax.Precision.HIGHEST, preferred_element_type=jnp.float32)
        distance = jnp.maximum(part_sq[:, None] + sqsum[None, :] - 2.0 * inner, 0.0)
        itself = (start + jnp.arange(block_rows, dtype=jnp.int32))[:, None] == all_ids[None, :]
        return distance, itself

    def gather_rows(values, start):
        return lax.dynamic_slice_in_dim(values, start, block_rows, 0)

    def stack_rows(result, width):
        return result.transpose(1, 0, 2).reshape(width, total)

    def nearest_fn(start):
        distance, itself = distances(start)
        return jnp.min(jnp.where(itself, jnp.inf, distance), axis=1)

    nearest = lax.map(nearest_fn, starts).reshape(total)

    def moment_fn(start):
        distance, itself = distances(start)
        shifted = distance - gather_rows(nearest, start)[:, None]
        expo = jnp.where(itself, 0.0, jnp.exp(-gather_rows(precision, start)[:, None] * shifted))
        return jnp.stack([jnp.sum(expo, axis=1), jnp.sum(expo * shifted, axis=1), jnp.sum(expo * shifted * shifted, axis=1)])

    moments = stack_rows(lax.map(moment_fn, starts), 3)
    calibrated = newton_update(moments[0], moments[1], moments[2], precision)

    def norm_fn(start):
        distance, itself = distances(start)
        shifted = distance - gather_rows(nearest, start)[:, None]
        return jnp.sum(jnp.where(itself, 0.0, jnp.exp(-gather_rows(calibrated, start)[:, None] * shifted)), axis=1)

    norm = lax.map(norm_fn, starts).reshape(total)

    def kernel_of(start, itself):
        part_y = lax.dynamic_slice_in_dim(embedding, start, block_rows, 1)
        delta_a = part_y[0][:, None] - embedding[0][None, :]
        delta_b = part_y[1][:, None] - embedding[1][None, :]
        return jnp.where(itself, 0.0, 1.0 / (1.0 + delta_a * delta_a + delta_b * delta_b)), part_y

    def qsum_fn(start):
        itself = (start + jnp.arange(block_rows, dtype=jnp.int32))[:, None] == all_ids[None, :]
        kernel, part_y = kernel_of(start, itself)
        return jnp.sum(kernel)

    qsum = jnp.sum(lax.map(qsum_fn, starts))

    def force_fn(start):
        distance, itself = distances(start)
        kernel, part_y = kernel_of(start, itself)
        cond_rows = jnp.exp(-gather_rows(calibrated, start)[:, None] * (distance - gather_rows(nearest, start)[:, None])) / gather_rows(norm, start)[:, None]
        cond_cols = jnp.exp(-calibrated[None, :] * (distance - nearest[None, :])) / norm[None, :]
        affinity = jnp.where(itself, 0.0, 0.5 * (cond_rows + cond_cols))
        coef = (affinity - total * kernel / qsum) * kernel
        pulled = jnp.dot(coef, embedding.T, precision=lax.Precision.HIGHEST, preferred_element_type=jnp.float32).T
        return part_y * jnp.sum(coef, axis=1)[None, :] - pulled

    force = stack_rows(lax.map(force_fn, starts), 2)
    return force, calibrated
```

```python
import math

import jax
import jax.numpy as jnp
from jax import lax
from jax.sharding import PartitionSpec as P

PERP = 30


def newton_update(zsum, first, second, start_prec):
    entropy = jnp.log(zsum) + start_prec * first / zsum
    spread = second / zsum - (first / zsum) ** 2
    factor = jnp.clip(
        (entropy - math.log(PERP)) / jnp.maximum(start_prec * start_prec * spread, 1.0), -2.0, 2.0
    )
    return start_prec * jnp.exp(factor)


def body(points, embedding, precision):
    per_dev = points.shape[1]
    width = points.shape[0]
    axes = ("row", "col")
    me = lax.axis_index("row") * lax.axis_size("col") + lax.axis_index("col")
    own_start = me * per_dev

    packed = jnp.concatenate([points, embedding], axis=0)
    every = lax.all_gather(packed, axes, axis=1, tiled=True)
    total = every.shape[1]
    all_coords = every[:width]
    all_map = every[width : width + 2]

    own_coords = points
    own_map = embedding
    own_sq = jnp.sum(own_coords * own_coords, axis=0)
    all_sq = jnp.sum(all_coords * all_coords, axis=0)

    inner = lax.dot_general(
        own_coords,
        all_coords,
        (((0,), (0,)), ((), ())),
        precision=lax.Precision.HIGHEST,
        preferred_element_type=jnp.float32,
    )
    distance = jnp.maximum(own_sq[:, None] + all_sq[None, :] - 2.0 * inner, 0.0)
    col_ids = jnp.arange(total, dtype=jnp.int32)[None, :]
    row_ids = (own_start + jnp.arange(per_dev, dtype=jnp.int32))[:, None]
    itself = row_ids == col_ids

    nearest = jnp.min(jnp.where(itself, jnp.inf, distance), axis=1)
    shifted = distance - nearest[:, None]
    expo = jnp.where(itself, 0.0, jnp.exp(-precision[:, None] * shifted))
    zsum = jnp.sum(expo, axis=1)
    first = jnp.sum(expo * shifted, axis=1)
    second = jnp.sum(expo * shifted * shifted, axis=1)
    calib = newton_update(zsum, first, second, precision)

    norm = jnp.sum(jnp.where(itself, 0.0, jnp.exp(-calib[:, None] * shifted)), axis=1)

    delta_a = own_map[0][:, None] - all_map[0][None, :]
    delta_b = own_map[1][:, None] - all_map[1][None, :]
    kernel = jnp.where(itself, 0.0, 1.0 / (1.0 + delta_a * delta_a + delta_b * delta_b))
    kernel_part = jnp.sum(kernel)

    qslot = jnp.where(jnp.arange(per_dev) == 0, kernel_part, 0.0)
    stats = jnp.stack([calib, nearest, 1.0 / norm, qslot])
    all_stats = lax.all_gather(stats, axes, axis=1, tiled=True)
    calib_cols = all_stats[0]
    nearest_cols = all_stats[1]
    inv_norm_cols = all_stats[2]
    qsum = jnp.sum(all_stats[3])

    cond_rows = jnp.exp(-calib[:, None] * shifted) * (1.0 / norm)[:, None]
    cond_cols = (
        jnp.exp(-calib_cols[None, :] * (distance - nearest_cols[None, :])) * inv_norm_cols[None, :]
    )
    affinity = jnp.where(itself, 0.0, 0.5 * (cond_rows + cond_cols))
    coef = (affinity - total * kernel / qsum) * kernel
    force = jnp.stack([jnp.sum(coef * delta_a, axis=1), jnp.sum(coef * delta_b, axis=1)])
    return (force, calib)


def solution(mesh):
    in_specs = (P(None, ("row", "col")), P(None, ("row", "col")), P(("row", "col")))
    out_specs = (P(None, ("row", "col")), P(("row", "col")))
    return jax.shard_map(body, mesh=mesh, in_specs=in_specs, out_specs=out_specs, check_vma=False)
```

```python
import math

import jax
import jax.numpy as jnp
from jax import lax
from jax.sharding import PartitionSpec as P

PERP = 30


def newton_update(zsum, first, second, start_prec):
    entropy = jnp.log(zsum) + start_prec * first / zsum
    spread = second / zsum - (first / zsum) ** 2
    factor = jnp.clip(
        (entropy - math.log(PERP)) / jnp.maximum(start_prec * start_prec * spread, 1.0), -2.0, 2.0
    )
    return start_prec * jnp.exp(factor)


def body(points, embedding, precision):
    per_dev = points.shape[1]
    width = points.shape[0]
    axes = ("row", "col")
    me = lax.axis_index("row") * lax.axis_size("col") + lax.axis_index("col")
    own_start = me * per_dev

    packed = jnp.concatenate([points, embedding], axis=0)
    every = lax.all_gather(lax.all_gather(packed, "col", axis=1, tiled=True), "row", axis=1, tiled=True)
    total = every.shape[1]
    all_coords = every[:width]
    all_map = every[width : width + 2]

    own_coords = points
    own_map = embedding
    own_sq = jnp.sum(own_coords * own_coords, axis=0)
    all_sq = jnp.sum(all_coords * all_coords, axis=0)

    inner = lax.dot_general(
        own_coords,
        all_coords,
        (((0,), (0,)), ((), ())),
        precision=lax.Precision.HIGHEST,
        preferred_element_type=jnp.float32,
    )
    distance = jnp.maximum(own_sq[:, None] + all_sq[None, :] - 2.0 * inner, 0.0)
    col_ids = jnp.arange(total, dtype=jnp.int32)[None, :]
    row_ids = (own_start + jnp.arange(per_dev, dtype=jnp.int32))[:, None]
    itself = row_ids == col_ids

    nearest = jnp.min(jnp.where(itself, jnp.inf, distance), axis=1)
    shifted = distance - nearest[:, None]
    expo = jnp.where(itself, 0.0, jnp.exp(-precision[:, None] * shifted))
    zsum = jnp.sum(expo, axis=1)
    first = jnp.sum(expo * shifted, axis=1)
    second = jnp.sum(expo * shifted * shifted, axis=1)
    calib = newton_update(zsum, first, second, precision)

    norm = jnp.sum(jnp.where(itself, 0.0, jnp.exp(-calib[:, None] * shifted)), axis=1)

    delta_a = own_map[0][:, None] - all_map[0][None, :]
    delta_b = own_map[1][:, None] - all_map[1][None, :]
    kernel = jnp.where(itself, 0.0, 1.0 / (1.0 + delta_a * delta_a + delta_b * delta_b))
    kernel_part = jnp.sum(kernel)

    qslot = jnp.where(jnp.arange(per_dev) == 0, kernel_part, 0.0)
    stats = jnp.stack([calib, nearest, 1.0 / norm, qslot])
    all_stats = lax.all_gather(lax.all_gather(stats, "col", axis=1, tiled=True), "row", axis=1, tiled=True)
    calib_cols = all_stats[0]
    nearest_cols = all_stats[1]
    inv_norm_cols = all_stats[2]
    qsum = jnp.sum(all_stats[3])

    cond_rows = jnp.exp(-calib[:, None] * shifted) * (1.0 / norm)[:, None]
    cond_cols = (
        jnp.exp(-calib_cols[None, :] * (distance - nearest_cols[None, :])) * inv_norm_cols[None, :]
    )
    affinity = jnp.where(itself, 0.0, 0.5 * (cond_rows + cond_cols))
    coef = (affinity - total * kernel / qsum) * kernel
    force = jnp.stack([jnp.sum(coef * delta_a, axis=1), jnp.sum(coef * delta_b, axis=1)])
    return (force, calib)


def solution(mesh):
    in_specs = (P(None, ("row", "col")), P(None, ("row", "col")), P(("row", "col")))
    out_specs = (P(None, ("row", "col")), P(("row", "col")))
    return jax.shard_map(body, mesh=mesh, in_specs=in_specs, out_specs=out_specs, check_vma=False)
```

```python
import math

import jax
import jax.numpy as jnp
from jax import lax
from jax.sharding import PartitionSpec as P

PERP = 30


def newton_update(zsum, first, second, start_prec):
    entropy = jnp.log(zsum) + start_prec * first / zsum
    spread = second / zsum - (first / zsum) ** 2
    factor = jnp.clip(
        (entropy - math.log(PERP)) / jnp.maximum(start_prec * start_prec * spread, 1.0), -2.0, 2.0
    )
    return start_prec * jnp.exp(factor)


def col_stage(values):
    count = lax.axis_size("col")
    parts = [values]
    for shift in range(1, count):
        pairs = [(i, (i + shift) % count) for i in range(count)]
        parts.append(lax.ppermute(values, "col", pairs))
    return jnp.concatenate(parts, axis=1)


def spread_all(values):
    return lax.all_gather(col_stage(values), "row", axis=1, tiled=True)


def body(points, embedding, precision):
    per_dev = points.shape[1]
    width = points.shape[0]
    axes = ("row", "col")
    own_start = lax.axis_index("row") * lax.axis_size("col") * per_dev

    own_coords = points
    own_map = embedding
    own_sq = jnp.sum(own_coords * own_coords, axis=0)
    packed = jnp.concatenate([points, embedding, own_sq[None, :]], axis=0)
    every = spread_all(packed)
    total = every.shape[1]
    all_coords = every[:width]
    all_map = every[width : width + 2]
    all_sq = every[width + 2]

    inner = lax.dot_general(
        own_coords,
        all_coords,
        (((0,), (0,)), ((), ())),
        precision=lax.Precision.HIGHEST,
        preferred_element_type=jnp.float32,
    )
    distance = jnp.maximum(own_sq[:, None] + all_sq[None, :] - 2.0 * inner, 0.0)
    col_ids = jnp.arange(total, dtype=jnp.int32)[None, :]
    row_ids = (own_start + jnp.arange(per_dev, dtype=jnp.int32))[:, None]
    itself = row_ids == col_ids

    nearest = jnp.min(jnp.where(itself, jnp.inf, distance), axis=1)
    shifted = distance - nearest[:, None]
    expo = jnp.where(itself, 0.0, jnp.exp(-precision[:, None] * shifted))
    zsum = jnp.sum(expo, axis=1)
    first = jnp.sum(expo * shifted, axis=1)
    second = jnp.sum(expo * shifted * shifted, axis=1)
    calib = newton_update(zsum, first, second, precision)

    norm = jnp.sum(jnp.where(itself, 0.0, jnp.exp(-calib[:, None] * shifted)), axis=1)

    delta_a = own_map[0][:, None] - all_map[0][None, :]
    delta_b = own_map[1][:, None] - all_map[1][None, :]
    kernel = jnp.where(itself, 0.0, 1.0 / (1.0 + delta_a * delta_a + delta_b * delta_b))
    kernel_part = jnp.sum(kernel)

    qslot = jnp.where(jnp.arange(per_dev) == 0, kernel_part, 0.0)
    stats = jnp.stack([calib, nearest, 1.0 / norm, qslot])
    all_stats = spread_all(stats)
    calib_cols = all_stats[0]
    nearest_cols = all_stats[1]
    inv_norm_cols = all_stats[2]
    qsum = jnp.sum(all_stats[3])

    cond_rows = jnp.exp(-calib[:, None] * shifted) * (1.0 / norm)[:, None]
    cond_cols = (
        jnp.exp(-calib_cols[None, :] * (distance - nearest_cols[None, :])) * inv_norm_cols[None, :]
    )
    affinity = jnp.where(itself, 0.0, 0.5 * (cond_rows + cond_cols))
    coef = (affinity - total * kernel / qsum) * kernel
    force = jnp.stack([jnp.sum(coef * delta_a, axis=1), jnp.sum(coef * delta_b, axis=1)])
    return (force, calib)


def solution(mesh):
    in_specs = (P(None, ("row", "col")), P(None, ("row", "col")), P(("row", "col")))
    out_specs = (P(None, ("row", "col")), P(("row", "col")))
    return jax.shard_map(body, mesh=mesh, in_specs=in_specs, out_specs=out_specs, check_vma=False)
```

```python
import math

import jax
import jax.numpy as jnp
from jax import lax
from jax.sharding import PartitionSpec as P

PERP = 30


def newton_update(zsum, first, second, start_prec):
    entropy = jnp.log(zsum) + start_prec * first / zsum
    spread = second / zsum - (first / zsum) ** 2
    factor = jnp.clip(
        (entropy - math.log(PERP)) / jnp.maximum(start_prec * start_prec * spread, 1.0), -2.0, 2.0
    )
    return start_prec * jnp.exp(factor)


def col_stage(values):
    count = lax.axis_size("col")
    parts = [values]
    for shift in range(1, count):
        pairs = [(i, (i + shift) % count) for i in range(count)]
        parts.append(lax.ppermute(values, "col", pairs))
    return jnp.concatenate(parts, axis=1)


def spread_all(values):
    return lax.all_gather(col_stage(values), "row", axis=1, tiled=True)


def body(points, embedding, precision):
    per_dev = points.shape[1]
    width = points.shape[0]
    axes = ("row", "col")
    own_start = lax.axis_index("row") * lax.axis_size("col") * per_dev

    own_coords = points
    own_map = embedding
    own_sq = jnp.sum(own_coords * own_coords, axis=0)
    packed = jnp.concatenate([points, embedding, own_sq[None, :]], axis=0)
    every = spread_all(packed)
    total = every.shape[1]
    all_coords = every[:width]
    all_map = every[width : width + 2]
    all_sq = every[width + 2]

    inner = lax.dot_general(
        own_coords,
        all_coords,
        (((0,), (0,)), ((), ())),
        precision=lax.Precision.HIGHEST,
        preferred_element_type=jnp.float32,
    )
    distance = jnp.maximum(own_sq[:, None] + all_sq[None, :] - 2.0 * inner, 0.0)
    col_ids = jnp.arange(total, dtype=jnp.int32)[None, :]
    row_ids = (own_start + jnp.arange(per_dev, dtype=jnp.int32))[:, None]
    itself = row_ids == col_ids

    nearest = jnp.min(jnp.where(itself, jnp.inf, distance), axis=1)
    shifted = distance - nearest[:, None]
    expo = jnp.where(itself, 0.0, jnp.exp(-precision[:, None] * shifted))
    zsum = jnp.sum(expo, axis=1)
    first = jnp.sum(expo * shifted, axis=1)
    second = jnp.sum(expo * shifted * shifted, axis=1)
    calib = newton_update(zsum, first, second, precision)

    row_expo = jnp.where(itself, 0.0, jnp.exp(-calib[:, None] * shifted))
    norm = jnp.sum(row_expo, axis=1)

    delta_a = own_map[0][:, None] - all_map[0][None, :]
    delta_b = own_map[1][:, None] - all_map[1][None, :]
    kernel = jnp.where(itself, 0.0, 1.0 / (1.0 + delta_a * delta_a + delta_b * delta_b))
    kernel_part = jnp.sum(kernel)
    row_pull = row_expo * kernel
    row_push = kernel * kernel
    pull_a = jnp.sum(row_pull * delta_a, axis=1)
    pull_b = jnp.sum(row_pull * delta_b, axis=1)
    push_a = jnp.sum(row_push * delta_a, axis=1)
    push_b = jnp.sum(row_push * delta_b, axis=1)

    qslot = jnp.where(jnp.arange(per_dev) == 0, kernel_part, 0.0)
    stats = jnp.stack([calib, nearest, 1.0 / norm, qslot])
    all_stats = spread_all(stats)
    calib_cols = all_stats[0]
    nearest_cols = all_stats[1]
    inv_norm_cols = all_stats[2]
    qsum = jnp.sum(all_stats[3])

    cond_cols = (
        jnp.exp(-calib_cols[None, :] * (distance - nearest_cols[None, :])) * inv_norm_cols[None, :]
    )
    col_pull = jnp.where(itself, 0.0, cond_cols) * kernel
    col_a = jnp.sum(col_pull * delta_a, axis=1)
    col_b = jnp.sum(col_pull * delta_b, axis=1)
    half_inv = 0.5 / norm
    scale = total / qsum
    force = jnp.stack(
        [
            half_inv * pull_a + 0.5 * col_a - scale * push_a,
            half_inv * pull_b + 0.5 * col_b - scale * push_b,
        ]
    )
    return (force, calib)


def solution(mesh):
    in_specs = (P(None, ("row", "col")), P(None, ("row", "col")), P(("row", "col")))
    out_specs = (P(None, ("row", "col")), P(("row", "col")))
    return jax.shard_map(body, mesh=mesh, in_specs=in_specs, out_specs=out_specs, check_vma=False)
```

```python
import math

import jax
import jax.numpy as jnp
from jax import lax
from jax.sharding import PartitionSpec as P

PERP = 30


def newton_update(zsum, first, second, start_prec):
    entropy = jnp.log(zsum) + start_prec * first / zsum
    spread = second / zsum - (first / zsum) ** 2
    factor = jnp.clip(
        (entropy - math.log(PERP)) / jnp.maximum(start_prec * start_prec * spread, 1.0), -2.0, 2.0
    )
    return start_prec * jnp.exp(factor)


def col_stage(values):
    count = lax.axis_size("col")
    parts = [values]
    for shift in range(1, count):
        pairs = [(i, (i + shift) % count) for i in range(count)]
        parts.append(lax.ppermute(values, "col", pairs))
    return jnp.concatenate(parts, axis=1)


def spread_all(values):
    return lax.all_gather(col_stage(values), "row", axis=1, tiled=True)


def body(points, embedding, precision):
    per_dev = points.shape[1]
    width = points.shape[0]
    axes = ("row", "col")
    own_start = lax.axis_index("row") * lax.axis_size("col") * per_dev

    own_coords = points
    own_map = embedding
    own_sq = jnp.sum(own_coords * own_coords, axis=0)
    packed = jnp.concatenate([points, embedding, own_sq[None, :]], axis=0)
    every = spread_all(packed)
    total = every.shape[1]
    all_coords = every[:width]
    all_map = every[width : width + 2]
    all_sq = every[width + 2]

    inner = lax.dot_general(
        own_coords,
        all_coords,
        (((0,), (0,)), ((), ())),
        precision=lax.Precision.HIGHEST,
        preferred_element_type=jnp.float32,
    )
    distance = jnp.maximum(own_sq[:, None] + all_sq[None, :] - 2.0 * inner, 0.0)
    col_ids = jnp.arange(total, dtype=jnp.int32)[None, :]
    row_ids = (own_start + jnp.arange(per_dev, dtype=jnp.int32))[:, None]
    itself = row_ids == col_ids

    nearest = jnp.min(jnp.where(itself, jnp.inf, distance), axis=1)
    shifted = distance - nearest[:, None]
    expo = jnp.where(itself, 0.0, jnp.exp(-precision[:, None] * shifted))
    zsum = jnp.sum(expo, axis=1)
    first = jnp.sum(expo * shifted, axis=1)
    second = jnp.sum(expo * shifted * shifted, axis=1)
    calib = newton_update(zsum, first, second, precision)

    norm = jnp.sum(jnp.where(itself, 0.0, jnp.exp(-calib[:, None] * shifted)), axis=1)

    delta_a = own_map[0][:, None] - all_map[0][None, :]
    delta_b = own_map[1][:, None] - all_map[1][None, :]
    kernel = jnp.where(itself, 0.0, 1.0 / (1.0 + delta_a * delta_a + delta_b * delta_b))
    kernel_part = jnp.sum(kernel)

    qslot = jnp.where(jnp.arange(per_dev) == 0, kernel_part, 0.0)
    half_inv = 0.5 / norm
    stats = jnp.stack([calib, nearest, half_inv, qslot])
    all_stats = spread_all(stats)
    calib_cols = all_stats[0]
    nearest_cols = all_stats[1]
    half_inv_cols = all_stats[2]
    qsum = jnp.sum(all_stats[3])
    scale = total / qsum

    cond_rows = jnp.exp(-calib[:, None] * shifted) * half_inv[:, None]
    cond_cols = (
        jnp.exp(-calib_cols[None, :] * (distance - nearest_cols[None, :])) * half_inv_cols[None, :]
    )
    affinity = jnp.where(itself, 0.0, cond_rows + cond_cols)
    coef = (affinity - scale * kernel) * kernel
    force = jnp.stack([jnp.sum(coef * delta_a, axis=1), jnp.sum(coef * delta_b, axis=1)])
    return (force, calib)


def solution(mesh):
    in_specs = (P(None, ("row", "col")), P(None, ("row", "col")), P(("row", "col")))
    out_specs = (P(None, ("row", "col")), P(("row", "col")))
    return jax.shard_map(body, mesh=mesh, in_specs=in_specs, out_specs=out_specs, check_vma=False)
```

```python
import math

import jax
import jax.numpy as jnp
from jax import lax
from jax.sharding import PartitionSpec as P

PERP = 30


def newton_update(zsum, first, second, start_prec):
    entropy = jnp.log(zsum) + start_prec * first / zsum
    spread = second / zsum - (first / zsum) ** 2
    factor = jnp.clip(
        (entropy - math.log(PERP)) / jnp.maximum(start_prec * start_prec * spread, 1.0), -2.0, 2.0
    )
    return start_prec * jnp.exp(factor)


def col_stage(values):
    count = lax.axis_size("col")
    parts = [values]
    for shift in range(1, count):
        pairs = [(i, (i + shift) % count) for i in range(count)]
        parts.append(lax.ppermute(values, "col", pairs))
    return jnp.concatenate(parts, axis=1)


def spread_all(values):
    return lax.all_gather(col_stage(values), "row", axis=1, tiled=True)


def body(points, embedding, precision):
    per_dev = points.shape[1]
    width = points.shape[0]
    axes = ("row", "col")
    own_start = lax.axis_index("row") * lax.axis_size("col") * per_dev

    own_coords = points
    own_map = embedding
    own_sq = jnp.sum(own_coords * own_coords, axis=0)
    packed = col_stage(jnp.concatenate([points, own_sq[None, :], embedding], axis=0))
    every = lax.all_gather(packed[: width + 1], "row", axis=1, tiled=True)
    all_map = lax.all_gather(packed[width + 1 :], "row", axis=1, tiled=True)
    total = every.shape[1]
    all_coords = every[:width]
    all_sq = every[width]

    inner = lax.dot_general(
        own_coords,
        all_coords,
        (((0,), (0,)), ((), ())),
        precision=lax.Precision.HIGHEST,
        preferred_element_type=jnp.float32,
    )
    distance = jnp.maximum(own_sq[:, None] + all_sq[None, :] - 2.0 * inner, 0.0)
    col_ids = jnp.arange(total, dtype=jnp.int32)[None, :]
    row_ids = (own_start + jnp.arange(per_dev, dtype=jnp.int32))[:, None]
    itself = row_ids == col_ids

    nearest = jnp.min(jnp.where(itself, jnp.inf, distance), axis=1)
    shifted = distance - nearest[:, None]
    expo = jnp.where(itself, 0.0, jnp.exp(-precision[:, None] * shifted))
    zsum = jnp.sum(expo, axis=1)
    first = jnp.sum(expo * shifted, axis=1)
    second = jnp.sum(expo * shifted * shifted, axis=1)
    calib = newton_update(zsum, first, second, precision)

    norm = jnp.sum(jnp.where(itself, 0.0, jnp.exp(-calib[:, None] * shifted)), axis=1)

    delta_a = own_map[0][:, None] - all_map[0][None, :]
    delta_b = own_map[1][:, None] - all_map[1][None, :]
    kernel = jnp.where(itself, 0.0, 1.0 / (1.0 + delta_a * delta_a + delta_b * delta_b))
    early_map, early_ids = lax.optimization_barrier((all_map, col_ids))
    early_a = own_map[0][:, None] - early_map[0][None, :]
    early_b = own_map[1][:, None] - early_map[1][None, :]
    kernel_part = jnp.sum(
        jnp.where(row_ids == early_ids, 0.0, 1.0 / (1.0 + early_a * early_a + early_b * early_b))
    )

    qslot = jnp.where(jnp.arange(per_dev) == 0, kernel_part, 0.0)
    stats = jnp.stack([calib, nearest, 1.0 / norm, qslot])
    all_stats = spread_all(stats)
    calib_cols = all_stats[0]
    nearest_cols = all_stats[1]
    inv_norm_cols = all_stats[2]
    qsum = jnp.sum(all_stats[3])

    cond_rows = jnp.exp(-calib[:, None] * shifted) * (1.0 / norm)[:, None]
    cond_cols = (
        jnp.exp(-calib_cols[None, :] * (distance - nearest_cols[None, :])) * inv_norm_cols[None, :]
    )
    affinity = jnp.where(itself, 0.0, 0.5 * (cond_rows + cond_cols))
    coef = (affinity - total * kernel / qsum) * kernel
    force = jnp.stack([jnp.sum(coef * delta_a, axis=1), jnp.sum(coef * delta_b, axis=1)])
    return (force, calib)


def solution(mesh):
    in_specs = (P(None, ("row", "col")), P(None, ("row", "col")), P(("row", "col")))
    out_specs = (P(None, ("row", "col")), P(("row", "col")))
    return jax.shard_map(body, mesh=mesh, in_specs=in_specs, out_specs=out_specs, check_vma=False)
```

```python
import math

import jax
import jax.numpy as jnp
from jax import lax
from jax.sharding import PartitionSpec as P

PERP = 30


def newton_update(zsum, first, second, start_prec):
    entropy = jnp.log(zsum) + start_prec * first / zsum
    spread = second / zsum - (first / zsum) ** 2
    factor = jnp.clip(
        (entropy - math.log(PERP)) / jnp.maximum(start_prec * start_prec * spread, 1.0), -2.0, 2.0
    )
    return start_prec * jnp.exp(factor)


def col_stage(values):
    count = lax.axis_size("col")
    held = values
    shift = 1
    while shift < count:
        pairs = [(i, (i + shift) % count) for i in range(count)]
        held = jnp.concatenate([held, lax.ppermute(held, "col", pairs)], axis=1)
        shift *= 2
    return held


def spread_all(values):
    return lax.all_gather(col_stage(values), "row", axis=1, tiled=True)


def body(points, embedding, precision):
    per_dev = points.shape[1]
    width = points.shape[0]
    axes = ("row", "col")
    own_start = lax.axis_index("row") * lax.axis_size("col") * per_dev

    own_coords = points
    own_map = embedding
    own_sq = jnp.sum(own_coords * own_coords, axis=0)
    packed = jnp.concatenate([points, embedding, own_sq[None, :]], axis=0)
    every = spread_all(packed)
    total = every.shape[1]
    all_coords = every[:width]
    all_map = every[width : width + 2]
    all_sq = every[width + 2]

    inner = lax.dot_general(
        own_coords,
        all_coords,
        (((0,), (0,)), ((), ())),
        precision=lax.Precision.HIGHEST,
        preferred_element_type=jnp.float32,
    )
    distance = jnp.maximum(own_sq[:, None] + all_sq[None, :] - 2.0 * inner, 0.0)
    col_ids = jnp.arange(total, dtype=jnp.int32)[None, :]
    row_ids = (own_start + jnp.arange(per_dev, dtype=jnp.int32))[:, None]
    itself = row_ids == col_ids

    nearest = jnp.min(jnp.where(itself, jnp.inf, distance), axis=1)
    shifted = distance - nearest[:, None]
    expo = jnp.where(itself, 0.0, jnp.exp(-precision[:, None] * shifted))
    zsum = jnp.sum(expo, axis=1)
    first = jnp.sum(expo * shifted, axis=1)
    second = jnp.sum(expo * shifted * shifted, axis=1)
    calib = newton_update(zsum, first, second, precision)

    norm = jnp.sum(jnp.where(itself, 0.0, jnp.exp(-calib[:, None] * shifted)), axis=1)

    delta_a = own_map[0][:, None] - all_map[0][None, :]
    delta_b = own_map[1][:, None] - all_map[1][None, :]
    kernel = jnp.where(itself, 0.0, 1.0 / (1.0 + delta_a * delta_a + delta_b * delta_b))
    kernel_part = jnp.sum(kernel)

    qslot = jnp.where(jnp.arange(per_dev) == 0, kernel_part, 0.0)
    stats = jnp.stack([calib, nearest, 1.0 / norm, qslot])
    all_stats = spread_all(stats)
    calib_cols = all_stats[0]
    nearest_cols = all_stats[1]
    inv_norm_cols = all_stats[2]
    qsum = jnp.sum(all_stats[3])

    cond_rows = jnp.exp(-calib[:, None] * shifted) * (1.0 / norm)[:, None]
    cond_cols = (
        jnp.exp(-calib_cols[None, :] * (distance - nearest_cols[None, :])) * inv_norm_cols[None, :]
    )
    affinity = jnp.where(itself, 0.0, 0.5 * (cond_rows + cond_cols))
    coef = (affinity - total * kernel / qsum) * kernel
    force = jnp.stack([jnp.sum(coef * delta_a, axis=1), jnp.sum(coef * delta_b, axis=1)])
    return (force, calib)


def solution(mesh):
    in_specs = (P(None, ("row", "col")), P(None, ("row", "col")), P(("row", "col")))
    out_specs = (P(None, ("row", "col")), P(("row", "col")))
    return jax.shard_map(body, mesh=mesh, in_specs=in_specs, out_specs=out_specs, check_vma=False)
```

```python
import math

import jax
import jax.numpy as jnp
from jax import lax
from jax.sharding import PartitionSpec as P

PERP = 30


def newton_update(zsum, first, second, start_prec):
    entropy = jnp.log(zsum) + start_prec * first / zsum
    spread = second / zsum - (first / zsum) ** 2
    factor = jnp.clip(
        (entropy - math.log(PERP)) / jnp.maximum(start_prec * start_prec * spread, 1.0), -2.0, 2.0
    )
    return start_prec * jnp.exp(factor)


def col_stage(values):
    count = lax.axis_size("col")
    held = values
    shift = 1
    while shift < count:
        pairs = [(i, (i + shift) % count) for i in range(count)]
        held = jnp.concatenate([held, lax.ppermute(held, "col", pairs)], axis=1)
        shift *= 2
    return held


def spread_all(values):
    return lax.all_gather(col_stage(values), "row", axis=1, tiled=True)


def body(points, embedding, precision):
    per_dev = points.shape[1]
    width = points.shape[0]
    axes = ("row", "col")
    own_start = lax.axis_index("row") * lax.axis_size("col") * per_dev

    own_coords = points
    own_map = embedding
    own_sq = jnp.sum(own_coords * own_coords, axis=0)
    packed = jnp.concatenate([points, embedding, own_sq[None, :]], axis=0)
    every = spread_all(packed)
    total = every.shape[1]
    all_coords = every[:width]
    all_map = every[width : width + 2]
    all_sq = every[width + 2]

    inner = lax.dot_general(
        own_coords,
        all_coords,
        (((0,), (0,)), ((), ())),
        precision=lax.Precision.HIGHEST,
        preferred_element_type=jnp.float32,
    )
    distance = jnp.maximum(own_sq[:, None] + all_sq[None, :] - 2.0 * inner, 0.0)
    col_ids = jnp.arange(total, dtype=jnp.int32)[None, :]
    row_ids = (own_start + jnp.arange(per_dev, dtype=jnp.int32))[:, None]
    itself = row_ids == col_ids

    nearest = jnp.min(jnp.where(itself, jnp.inf, distance), axis=1)
    shifted = distance - nearest[:, None]
    expo = jnp.where(itself, 0.0, jnp.exp(-precision[:, None] * shifted))
    zsum = jnp.sum(expo, axis=1)
    first = jnp.sum(expo * shifted, axis=1)
    second = jnp.sum(expo * shifted * shifted, axis=1)
    calib = newton_update(zsum, first, second, precision)

    norm = jnp.sum(jnp.where(itself, 0.0, jnp.exp(-calib[:, None] * shifted)), axis=1)

    delta_a = own_map[0][:, None] - all_map[0][None, :]
    delta_b = own_map[1][:, None] - all_map[1][None, :]
    kernel = jnp.where(itself, 0.0, 1.0 / (1.0 + delta_a * delta_a + delta_b * delta_b))
    kernel_part = jnp.sum(kernel)

    qslot = jnp.where(jnp.arange(per_dev) == 0, kernel_part, 0.0)
    stats = jnp.stack([calib, nearest, 1.0 / norm, qslot])
    held = col_stage(stats)
    rows = lax.axis_size("row")
    shift = 1
    while shift < rows:
        pairs = [(i, (i + shift) % rows) for i in range(rows)]
        held = jnp.concatenate([held, lax.ppermute(held, "row", pairs)], axis=1)
        shift *= 2
    blocks = held.reshape(held.shape[0], rows, -1)[:, ::-1]
    all_stats = jnp.roll(blocks, lax.axis_index("row") + 1, axis=1).reshape(held.shape)
    calib_cols = all_stats[0]
    nearest_cols = all_stats[1]
    inv_norm_cols = all_stats[2]
    qsum = jnp.sum(all_stats[3])

    cond_rows = jnp.exp(-calib[:, None] * shifted) * (1.0 / norm)[:, None]
    cond_cols = (
        jnp.exp(-calib_cols[None, :] * (distance - nearest_cols[None, :])) * inv_norm_cols[None, :]
    )
    affinity = jnp.where(itself, 0.0, 0.5 * (cond_rows + cond_cols))
    coef = (affinity - total * kernel / qsum) * kernel
    force = jnp.stack([jnp.sum(coef * delta_a, axis=1), jnp.sum(coef * delta_b, axis=1)])
    return (force, calib)


def solution(mesh):
    in_specs = (P(None, ("row", "col")), P(None, ("row", "col")), P(("row", "col")))
    out_specs = (P(None, ("row", "col")), P(("row", "col")))
    return jax.shard_map(body, mesh=mesh, in_specs=in_specs, out_specs=out_specs, check_vma=False)
```
